256 devices in a mesh: lat: 16 (over z, core), elev: 16 (over y, x).
Axes of the slice: x: 4, y: 4, z: 8, core: 2. Of those that a mesh axis runs over, the one named last changes fastest.
Arguments:
- volume: bfloat16 [128, 128, 128, 256], P('lat', 'elev'), may hold values from -64 to 64
- lat_taps: float32 [7], replicated, may hold values from 0.05 to 0.3
- elev_taps: float32 [7], replicated, may hold values from 0.05 to 0.3
- time_taps: bfloat16 [32], replicated, may hold values from -3 to 3
- clutter_rank: int32 [], replicated, may hold values from 4 to 32
- noise_rank: int32 [], replicated, may hold values from 128 to 256
Outputs:
- cleaned: bfloat16 [128, 128, 128, 256], P('lat', 'elev')
- power: float32 [128, 128, 128], P('lat', 'elev')
- band_weights: float32 [256, 256], replicated
The draws below stay inside these ranges and needn't reach their ends.
All inputs are finite; a program needn't handle non-finite values.
Results may differ from the reference program's by a relative error of at most 0.0034.
The reference program's roundings to bfloat16 on the way count: a program that leaves them out, or rounds other values in their place, can miss the bound.
Values may be sent and summed in bfloat16 or wider, within the bound.
No kernel may reach another device: no remote copies, remote signals or barrier semaphores. Data moves between devices by JAX's collectives and lax.ppermute only.
A program may use at most 64 MiB of HBM per device.

```python
import math
import jax
import jax.numpy as jnp
from jax import lax

C = 256
LB = 8
AX = 128
TAPS_S = 7
TAPS_T = 32
NL = 128
NE = 128
N_LAT = 16


def draw_volume(key, part):
    key_base = jax.random.fold_in(key, 11)
    keys_all = jax.random.split(key_base, 7)
    shape_all = (NL, NE, AX, C)
    grid_side = 4
    lat_index = jnp.arange(NL, dtype=jnp.int32)
    elev_index = jnp.arange(NE, dtype=jnp.int32)
    lat_pos = lat_index.astype(jnp.float32) / max(NL - 1, 1)
    elev_pos = elev_index.astype(jnp.float32) / max(NE - 1, 1)
    rising = jnp.sqrt((1.0 + 2.0 * lat_pos)[:, None, None, None] * (1.0 + 2.0 * elev_pos)[None, :, None, None])
    region_lat = lat_index * grid_side // NL
    region_elev = elev_index * grid_side // NE
    region_ids = region_lat[:, None] * grid_side + region_elev[None, :]
    region_vectors = jax.random.normal(keys_all[4], (grid_side * grid_side, C), jnp.float32)
    region_strength = jnp.exp(jax.random.uniform(keys_all[5], (grid_side * grid_side,), jnp.float32, math.log(1.5), math.log(6.0)))
    voxel_vectors = region_vectors[region_ids]
    voxel_strength = region_strength[region_ids]
    column_scale = jnp.exp(jax.random.uniform(keys_all[2], (C,), jnp.float32, math.log(0.3), math.log(3.0)))
    row_scale = jnp.exp(jax.random.uniform(keys_all[1], (NL, NE, AX, 1), jnp.float32, math.log(0.3), math.log(3.0)))
    noise_values = jnp.clip(jax.random.normal(keys_all[0], shape_all, jnp.float32), -6.0, 6.0)
    amplitude = jnp.clip(jax.random.normal(keys_all[6], (NL, NE, AX, 1), jnp.float32), -4.0, 4.0)
    noise_part = 0.5 * noise_values * row_scale * column_scale
    clutter_part = voxel_strength[:, :, None, None] * amplitude * voxel_vectors[:, :, None, :]
    values = jnp.clip((noise_part + clutter_part) * rising, -64.0, 64.0)
    values = values.at[0, 0, 0, 0].set(64.0)
    values = values.at[NL - 1, NE - 1, AX - 1, C - 1].set(-64.0)
    return values.astype(jnp.bfloat16)


def normal_values(own_key, dims, scale, bound, kind=jnp.bfloat16):
    return jnp.clip(scale * jax.random.normal(own_key, dims, jnp.float32), -bound, bound).astype(kind)


def setup_inputs(seed: int = 0) -> dict:
    splits = jax.random.split(jax.random.key(seed), 7)
    volume = draw_volume(jax.random.fold_in(splits[6], 71), 0)
    lat_taps = jnp.clip(jax.random.uniform(splits[1], (TAPS_S,), jnp.float32, 0.05, 0.3), 0.05, 0.3)
    elev_taps = jnp.clip(jax.random.uniform(splits[2], (TAPS_S,), jnp.float32, 0.05, 0.3), 0.05, 0.3)
    time_taps = normal_values(splits[3], (TAPS_T,), 0.2, 3.0)
    clutter_rank = jax.random.randint(splits[4], (), 4, C // 8 + 1).astype(jnp.int32)
    noise_rank = jax.random.randint(splits[5], (), C // 2, C + 1).astype(jnp.int32)
    return dict(volume=volume, lat_taps=lat_taps, elev_taps=elev_taps, time_taps=time_taps, clutter_rank=clutter_rank, noise_rank=noise_rank)


def time_matrix(time_taps, frames):
    count_taps = time_taps.shape[0]
    source = jnp.arange(frames, dtype=jnp.int32)[:, None]
    target = jnp.arange(frames, dtype=jnp.int32)[None, :]
    lagged = target - source
    matched = lagged[:, :, None] == jnp.arange(count_taps, dtype=jnp.int32)[None, None, :]
    single = lax.optimization_barrier(jnp.sum(jnp.where(matched, time_taps.astype(jnp.float32)[None, None, :], jnp.float32(0.0)), axis=2))
    paired = jnp.kron(jnp.eye(2, dtype=jnp.float32), single)
    return paired.astype(jnp.bfloat16)

def smooth(extended, lat_taps, elev_taps, lat_count, elev_count):
    lat_sum = lat_taps[0] * extended[0:lat_count].astype(jnp.float32)
    for index_tap in range(1, 7):
        lat_sum = lat_sum + lat_taps[index_tap] * extended[index_tap:index_tap + lat_count].astype(jnp.float32)
    result = elev_taps[0] * lat_sum[:, 0:elev_count]
    for index_tap in range(1, 7):
        result = result + elev_taps[index_tap] * lat_sum[:, index_tap:index_tap + elev_count]
    return result

def filtered_rows(extended, lat_taps, elev_taps, matrix, lat_count, elev_count):
    smoothed = smooth(extended, lat_taps, elev_taps, lat_count, elev_count).astype(jnp.bfloat16)
    flat_rows = smoothed.reshape(-1, matrix.shape[0])
    return jnp.dot(flat_rows.astype(jnp.float32), matrix.astype(jnp.float32), preferred_element_type=jnp.float32).astype(jnp.bfloat16)

def band_filter(gram_sum, clutter_rank, noise_rank):
    width = gram_sum.shape[0]
    identity = jnp.eye(width, dtype=jnp.float32)
    total_trace = jnp.sum(gram_sum * identity)

    def resolvent(rank_value):
        level = total_trace / rank_value.astype(jnp.float32)
        factor = jnp.linalg.cholesky(gram_sum + level * identity)
        solved = lax.linalg.triangular_solve(factor, jnp.sqrt(level) * identity, left_side=True, lower=True)
        return jnp.dot(solved.T, solved, precision=lax.Precision.HIGHEST)
    return resolvent(clutter_rank) - resolvent(noise_rank)

def reference(volume, lat_taps, elev_taps, time_taps, clutter_rank, noise_rank):
    padded = jnp.pad(volume, ((3, 3), (3, 3), (0, 0), (0, 0)))
    matrix = time_matrix(time_taps, C // 2)
    starts = jnp.arange(N_LAT, dtype=jnp.int32) * LB

    def block_rows(start):
        anchor = jnp.zeros((), jnp.int32)
        extended = lax.dynamic_slice(padded, (start, anchor, anchor, anchor), (LB + 6, NE + 6, AX, C))
        return filtered_rows(extended, lat_taps, elev_taps, matrix, LB, NE)

    def accumulate(carry, start):
        row_block = block_rows(start)
        product = lax.dot_general(row_block.astype(jnp.float32), row_block.astype(jnp.float32), (((0,), (0,)), ((), ())), preferred_element_type=jnp.float32)
        return (carry + product, None)
    gram_sum, _ = lax.scan(accumulate, jnp.zeros((C, C), jnp.float32), starts)
    weights = band_filter(gram_sum, clutter_rank, noise_rank)
    weights_low = weights.astype(jnp.bfloat16)

    def output_block(start):
        row_block = block_rows(start)
        return jnp.dot(row_block.astype(jnp.float32), weights_low.astype(jnp.float32), preferred_element_type=jnp.float32).astype(jnp.bfloat16)
    blocks_out = lax.map(output_block, starts)
    cleaned = blocks_out.reshape(NL, NE, AX, C)
    power = lax.optimization_barrier(jnp.sum(jnp.square(cleaned.astype(jnp.float32)), axis=3))
    return (cleaned, power, weights)
```

```python
import jax
import jax.numpy as jnp
from jax import lax
from jax.sharding import PartitionSpec as P


def padded(block, sides, width):
    for axis, dim in sides:
        count = lax.axis_size(axis)
        forward = [(i, i + 1) for i in range(count - 1)]
        backward = [(target, source) for source, target in forward]
        low = lax.ppermute(
            lax.slice_in_dim(block, block.shape[dim] - width, None, axis=dim), axis, forward
        )
        high = lax.ppermute(lax.slice_in_dim(block, 0, width, axis=dim), axis, backward)
        block = jnp.concatenate([low, block, high], axis=dim)
    return block


def time_matrix(time_taps, frames):
    count_taps = time_taps.shape[0]
    source = jnp.arange(frames, dtype=jnp.int32)[:, None]
    target = jnp.arange(frames, dtype=jnp.int32)[None, :]
    lagged = target - source
    matched = lagged[:, :, None] == jnp.arange(count_taps, dtype=jnp.int32)[None, None, :]
    single = jnp.sum(
        jnp.where(matched, time_taps.astype(jnp.float32)[None, None, :], jnp.float32(0.0)), axis=2
    )
    paired = jnp.kron(jnp.eye(2, dtype=jnp.float32), single)
    return paired.astype(jnp.bfloat16)


def smooth(extended, lat_taps, elev_taps, lat_count, elev_count):
    lat_sum = lat_taps[0] * extended[0:lat_count].astype(jnp.float32)
    for index_tap in range(1, 7):
        lat_sum = lat_sum + lat_taps[index_tap] * extended[
            index_tap : index_tap + lat_count
        ].astype(jnp.float32)
    result = elev_taps[0] * lat_sum[:, 0:elev_count]
    for index_tap in range(1, 7):
        result = result + elev_taps[index_tap] * lat_sum[:, index_tap : index_tap + elev_count]
    return result


def filtered_rows(extended, lat_taps, elev_taps, matrix, lat_count, elev_count):
    smoothed = smooth(extended, lat_taps, elev_taps, lat_count, elev_count).astype(jnp.bfloat16)
    flat_rows = smoothed.reshape(-1, matrix.shape[0])
    return jnp.dot(flat_rows, matrix, preferred_element_type=jnp.float32).astype(jnp.bfloat16)


def butterfly_sum(block):
    for axis in ("lat", "elev"):
        count = lax.axis_size(axis)
        stride = 1
        while stride < count:
            pairs = [(i, i ^ stride) for i in range(count)]
            block = block + lax.ppermute(block, axis, pairs)
            stride *= 2
    return block


def packed_gram_sum(gram):
    half = gram.shape[0] // 2
    upper = gram[:half, :half]
    side = gram[:half, half:]
    lower = gram[half:, half:]
    row = jnp.arange(half, dtype=jnp.int32)[:, None]
    col = jnp.arange(half, dtype=jnp.int32)[None, :]
    keep_upper = row <= col
    merged = jnp.where(keep_upper, upper, lower)
    diagonal = jnp.diagonal(lower)[None, :]
    packed = butterfly_sum(jnp.concatenate([side, merged, diagonal], axis=0))
    side = packed[:half]
    merged = packed[half : 2 * half]
    diagonal = packed[2 * half]
    upper = jnp.where(keep_upper, merged, merged.T)
    lower = jnp.where(row > col, merged, merged.T)
    lower = jnp.where(row == col, diagonal[None, :], lower)
    return jnp.concatenate(
        [jnp.concatenate([upper, side], axis=1), jnp.concatenate([side.T, lower], axis=1)], axis=0
    )


def band_filter(gram_sum, clutter_rank, noise_rank, steps=13):
    width = gram_sum.shape[0]
    identity = jnp.eye(width, dtype=jnp.float32)
    total_trace = jnp.sum(gram_sum * identity)
    levels = total_trace / jnp.stack([clutter_rank, noise_rank]).astype(jnp.float32)
    shifted = gram_sum[None] + levels[:, None, None] * identity[None]
    scale = 2.0 / (2.0 * levels + total_trace)
    inverse = scale[:, None, None] * identity[None]
    for _ in range(steps):
        product = jnp.einsum("bij,bjk->bik", shifted, inverse, precision=lax.Precision.HIGHEST)
        inverse = 2.0 * inverse - jnp.einsum(
            "bij,bjk->bik", inverse, product, precision=lax.Precision.HIGHEST
        )
    resolvents = levels[:, None, None] * inverse
    return resolvents[0] - resolvents[1]


def body(volume, lat_taps, elev_taps, time_taps, clutter_rank, noise_rank):
    lat_count, elev_count, depth, columns = volume.shape
    matrix = time_matrix(time_taps, columns // 2)
    extended = padded(volume, (("lat", 0), ("elev", 1)), 3)
    row_block = filtered_rows(extended, lat_taps, elev_taps, matrix, lat_count, elev_count)
    local_gram = lax.dot_general(
        row_block, row_block, (((0,), (0,)), ((), ())), preferred_element_type=jnp.float32
    )
    gram_sum = packed_gram_sum(local_gram)
    weights = band_filter(gram_sum, clutter_rank, noise_rank)
    cleaned_rows = jnp.dot(
        row_block, weights.astype(jnp.bfloat16), preferred_element_type=jnp.float32
    ).astype(jnp.bfloat16)
    cleaned = cleaned_rows.reshape(lat_count, elev_count, depth, columns)
    power = jnp.sum(jnp.square(cleaned.astype(jnp.float32)), axis=3)
    return (cleaned, power, weights)


def solution(mesh):
    placed = (P("lat", "elev", None, None), P(), P(), P(), P(), P())
    return jax.shard_map(
        body,
        mesh=mesh,
        in_specs=placed,
        out_specs=(P("lat", "elev", None, None), P("lat", "elev", None), P()),
        check_vma=False,
    )
```

```python
import jax
import jax.numpy as jnp
from jax import lax
from jax.sharding import PartitionSpec as P


def halo_pieces(block, width):
    lat_count = lax.axis_size("lat")
    elev_count = lax.axis_size("elev")
    lat_size, elev_size = block.shape[0], block.shape[1]
    low_lat = slice(lat_size - width, lat_size)
    high_lat = slice(0, width)
    low_elev = slice(elev_size - width, elev_size)
    high_elev = slice(0, width)

    def shift(piece, axis, step):
        count = lax.axis_size(axis)
        pairs = [(i, i + step) for i in range(count) if 0 <= i + step < count]
        return lax.ppermute(piece, axis, pairs)

    def shift_both(piece, lat_step, elev_step):
        pairs = []
        for i in range(lat_count):
            for j in range(elev_count):
                ti, tj = i + lat_step, j + elev_step
                if 0 <= ti < lat_count and 0 <= tj < elev_count:
                    pairs.append((i * elev_count + j, ti * elev_count + tj))
        return lax.ppermute(piece, ("lat", "elev"), pairs)

    north = shift(block[low_lat], "lat", 1)
    south = shift(block[high_lat], "lat", -1)
    west = shift(block[:, low_elev], "elev", 1)
    east = shift(block[:, high_elev], "elev", -1)
    north_west = shift_both(block[low_lat, low_elev], 1, 1)
    north_east = shift_both(block[low_lat, high_elev], 1, -1)
    south_west = shift_both(block[high_lat, low_elev], -1, 1)
    south_east = shift_both(block[high_lat, high_elev], -1, -1)
    top = jnp.concatenate([north_west, north, north_east], axis=1)
    middle = jnp.concatenate([west, block, east], axis=1)
    bottom = jnp.concatenate([south_west, south, south_east], axis=1)
    return jnp.concatenate([top, middle, bottom], axis=0)


def band_taps(taps, count, width):
    out_index = jnp.arange(count, dtype=jnp.int32)[:, None]
    in_index = jnp.arange(count + 2 * width, dtype=jnp.int32)[None, :]
    lag = in_index - out_index
    matched = lag[:, :, None] == jnp.arange(taps.shape[0], dtype=jnp.int32)[None, None, :]
    return jnp.sum(jnp.where(matched, taps[None, None, :], jnp.float32(0.0)), axis=2)


def time_matrix(time_taps, frames):
    count_taps = time_taps.shape[0]
    source = jnp.arange(frames, dtype=jnp.int32)[:, None]
    target = jnp.arange(frames, dtype=jnp.int32)[None, :]
    lagged = target - source
    matched = lagged[:, :, None] == jnp.arange(count_taps, dtype=jnp.int32)[None, None, :]
    single = jnp.sum(
        jnp.where(matched, time_taps.astype(jnp.float32)[None, None, :], jnp.float32(0.0)), axis=2
    )
    paired = jnp.kron(jnp.eye(2, dtype=jnp.float32), single)
    return paired.astype(jnp.bfloat16)


def filtered_rows(extended, lat_taps, elev_taps, matrix, lat_count, elev_count):
    weights = jnp.kron(band_taps(lat_taps, lat_count, 3), band_taps(elev_taps, elev_count, 3))
    sources = extended.reshape(weights.shape[1], -1).astype(jnp.float32)
    smoothed = jnp.dot(
        weights, sources, precision=lax.Precision.HIGH, preferred_element_type=jnp.float32
    ).astype(jnp.bfloat16)
    flat_rows = smoothed.reshape(-1, matrix.shape[0])
    return jnp.dot(flat_rows, matrix, preferred_element_type=jnp.float32).astype(jnp.bfloat16)


def butterfly_sum(block):
    for axis in ("lat", "elev"):
        count = lax.axis_size(axis)
        stride = 1
        while stride < count:
            pairs = [(i, i ^ stride) for i in range(count)]
            block = block + lax.ppermute(block, axis, pairs)
            stride *= 2
    return block


def packed_gram_sum(gram):
    half = gram.shape[0] // 2
    upper = gram[:half, :half]
    side = gram[:half, half:]
    lower = gram[half:, half:]
    row = jnp.arange(half, dtype=jnp.int32)[:, None]
    col = jnp.arange(half, dtype=jnp.int32)[None, :]
    keep_upper = row <= col
    merged = jnp.where(keep_upper, upper, lower)
    diagonal = jnp.diagonal(lower)[None, :]
    packed = butterfly_sum(jnp.concatenate([side, merged, diagonal], axis=0))
    side = packed[:half]
    merged = packed[half : 2 * half]
    diagonal = packed[2 * half]
    upper = jnp.where(keep_upper, merged, merged.T)
    lower = jnp.where(row > col, merged, merged.T)
    lower = jnp.where(row == col, diagonal[None, :], lower)
    return jnp.concatenate(
        [jnp.concatenate([upper, side], axis=1), jnp.concatenate([side.T, lower], axis=1)], axis=0
    )


def band_filter(gram_sum, clutter_rank, noise_rank, steps=13):
    width = gram_sum.shape[0]
    identity = jnp.eye(width, dtype=jnp.float32)
    total_trace = jnp.sum(gram_sum * identity)
    levels = total_trace / jnp.stack([clutter_rank, noise_rank]).astype(jnp.float32)
    shifted = gram_sum[None] + levels[:, None, None] * identity[None]
    scale = 2.0 / (2.0 * levels + total_trace)
    inverse = scale[:, None, None] * identity[None]
    for _ in range(steps):
        product = jnp.einsum("bij,bjk->bik", shifted, inverse, precision=lax.Precision.HIGHEST)
        inverse = 2.0 * inverse - jnp.einsum(
            "bij,bjk->bik", inverse, product, precision=lax.Precision.HIGHEST
        )
    resolvents = levels[:, None, None] * inverse
    return resolvents[0] - resolvents[1]


def body(volume, lat_taps, elev_taps, time_taps, clutter_rank, noise_rank):
    lat_count, elev_count, depth, columns = volume.shape
    matrix = time_matrix(time_taps, columns // 2)
    extended = halo_pieces(volume, 3)
    row_block = filtered_rows(extended, lat_taps, elev_taps, matrix, lat_count, elev_count)
    local_gram = lax.dot_general(
        row_block, row_block, (((0,), (0,)), ((), ())), preferred_element_type=jnp.float32
    )
    gram_sum = packed_gram_sum(local_gram)
    weights = band_filter(gram_sum, clutter_rank, noise_rank)
    cleaned_rows = jnp.dot(
        row_block, weights.astype(jnp.bfloat16), preferred_element_type=jnp.float32
    ).astype(jnp.bfloat16)
    cleaned = cleaned_rows.reshape(lat_count, elev_count, depth, columns)
    power = jnp.sum(jnp.square(cleaned.astype(jnp.float32)), axis=3)
    return (cleaned, power, weights)


def solution(mesh):
    placed = (P("lat", "elev", None, None), P(), P(), P(), P(), P())
    return jax.shard_map(
        body,
        mesh=mesh,
        in_specs=placed,
        out_specs=(P("lat", "elev", None, None), P("lat", "elev", None), P()),
        check_vma=False,
    )
```

```python
import jax
import jax.numpy as jnp
from jax import lax
from jax.sharding import PartitionSpec as P


def halo_pieces(block, width):
    lat_size, elev_size = block.shape[0], block.shape[1]
    low_lat = slice(lat_size - width, lat_size)
    high_lat = slice(0, width)
    low_elev = slice(elev_size - width, elev_size)
    high_elev = slice(0, width)

    def shift(piece, axis, step):
        count = lax.axis_size(axis)
        pairs = [(i, i + step) for i in range(count) if 0 <= i + step < count]
        return lax.ppermute(piece, axis, pairs)

    north = shift(block[low_lat], "lat", 1)
    south = shift(block[high_lat], "lat", -1)
    west = shift(block[:, low_elev], "elev", 1)
    east = shift(block[:, high_elev], "elev", -1)
    north_west = shift(west[low_lat], "lat", 1)
    north_east = shift(east[low_lat], "lat", 1)
    south_west = shift(west[high_lat], "lat", -1)
    south_east = shift(east[high_lat], "lat", -1)
    top = jnp.concatenate([north_west, north, north_east], axis=1)
    middle = jnp.concatenate([west, block, east], axis=1)
    bottom = jnp.concatenate([south_west, south, south_east], axis=1)
    return jnp.concatenate([top, middle, bottom], axis=0)


def time_matrix(time_taps, frames):
    count_taps = time_taps.shape[0]
    source = jnp.arange(frames, dtype=jnp.int32)[:, None]
    target = jnp.arange(frames, dtype=jnp.int32)[None, :]
    lagged = target - source
    matched = lagged[:, :, None] == jnp.arange(count_taps, dtype=jnp.int32)[None, None, :]
    single = jnp.sum(
        jnp.where(matched, time_taps.astype(jnp.float32)[None, None, :], jnp.float32(0.0)), axis=2
    )
    paired = jnp.kron(jnp.eye(2, dtype=jnp.float32), single)
    return paired.astype(jnp.bfloat16)


def smooth(extended, lat_taps, elev_taps, lat_count, elev_count):
    lat_sum = lat_taps[0] * extended[0:lat_count].astype(jnp.float32)
    for index_tap in range(1, 7):
        lat_sum = lat_sum + lat_taps[index_tap] * extended[
            index_tap : index_tap + lat_count
        ].astype(jnp.float32)
    result = elev_taps[0] * lat_sum[:, 0:elev_count]
    for index_tap in range(1, 7):
        result = result + elev_taps[index_tap] * lat_sum[:, index_tap : index_tap + elev_count]
    return result


def filtered_rows(extended, lat_taps, elev_taps, matrix, lat_count, elev_count):
    smoothed = smooth(extended, lat_taps, elev_taps, lat_count, elev_count).astype(jnp.bfloat16)
    flat_rows = smoothed.reshape(-1, matrix.shape[0])
    return jnp.dot(flat_rows, matrix, preferred_element_type=jnp.float32).astype(jnp.bfloat16)


def butterfly_sum(block):
    for axis in ("lat", "elev"):
        count = lax.axis_size(axis)
        stride = 1
        while stride < count:
            pairs = [(i, i ^ stride) for i in range(count)]
            block = block + lax.ppermute(block, axis, pairs)
            stride *= 2
    return block


def packed_gram_sum(gram):
    half = gram.shape[0] // 2
    upper = gram[:half, :half]
    side = gram[:half, half:]
    lower = gram[half:, half:]
    row = jnp.arange(half, dtype=jnp.int32)[:, None]
    col = jnp.arange(half, dtype=jnp.int32)[None, :]
    keep_upper = row <= col
    merged = jnp.where(keep_upper, upper, lower)
    diagonal = jnp.diagonal(lower)[None, :]
    packed = butterfly_sum(jnp.concatenate([side, merged, diagonal], axis=0))
    side = packed[:half]
    merged = packed[half : 2 * half]
    diagonal = packed[2 * half]
    upper = jnp.where(keep_upper, merged, merged.T)
    lower = jnp.where(row > col, merged, merged.T)
    lower = jnp.where(row == col, diagonal[None, :], lower)
    return jnp.concatenate(
        [jnp.concatenate([upper, side], axis=1), jnp.concatenate([side.T, lower], axis=1)], axis=0
    )


def band_filter(gram_sum, clutter_rank, noise_rank, steps=13):
    width = gram_sum.shape[0]
    identity = jnp.eye(width, dtype=jnp.float32)
    total_trace = jnp.sum(gram_sum * identity)
    levels = total_trace / jnp.stack([clutter_rank, noise_rank]).astype(jnp.float32)
    shifted = gram_sum[None] + levels[:, None, None] * identity[None]
    scale = 2.0 / (2.0 * levels + total_trace)
    inverse = scale[:, None, None] * identity[None]

    def refine(_, inverse):
        product = jnp.einsum("bij,bjk->bik", shifted, inverse, precision=lax.Precision.HIGHEST)
        return 2.0 * inverse - jnp.einsum(
            "bij,bjk->bik", inverse, product, precision=lax.Precision.HIGHEST
        )

    inverse = lax.fori_loop(0, steps, refine, inverse)
    resolvents = levels[:, None, None] * inverse
    return resolvents[0] - resolvents[1]


def body(volume, lat_taps, elev_taps, time_taps, clutter_rank, noise_rank):
    lat_count, elev_count, depth, columns = volume.shape
    matrix = time_matrix(time_taps, columns // 2)
    extended = halo_pieces(volume, 3)
    row_block = filtered_rows(extended, lat_taps, elev_taps, matrix, lat_count, elev_count)
    local_gram = lax.dot_general(
        row_block, row_block, (((0,), (0,)), ((), ())), preferred_element_type=jnp.float32
    )
    gram_sum = packed_gram_sum(local_gram)
    weights = band_filter(gram_sum, clutter_rank, noise_rank)
    cleaned_rows = jnp.dot(
        row_block, weights.astype(jnp.bfloat16), preferred_element_type=jnp.float32
    ).astype(jnp.bfloat16)
    cleaned = cleaned_rows.reshape(lat_count, elev_count, depth, columns)
    power = jnp.sum(jnp.square(cleaned.astype(jnp.float32)), axis=3)
    return (cleaned, power, weights)


def solution(mesh):
    placed = (P("lat", "elev", None, None), P(), P(), P(), P(), P())
    return jax.shard_map(
        body,
        mesh=mesh,
        in_specs=placed,
        out_specs=(P("lat", "elev", None, None), P("lat", "elev", None), P()),
        check_vma=False,
    )
```

```python
import jax
import jax.numpy as jnp
from jax import lax
from jax.sharding import PartitionSpec as P


def halo_pieces(block, width):
    lat_size, elev_size = block.shape[0], block.shape[1]
    low_lat = slice(lat_size - width, lat_size)
    high_lat = slice(0, width)
    low_elev = slice(elev_size - width, elev_size)
    high_elev = slice(0, width)

    def shift(piece, axis, step):
        count = lax.axis_size(axis)
        pairs = [(i, i + step) for i in range(count) if 0 <= i + step < count]
        return lax.ppermute(piece, axis, pairs)

    north = shift(block[low_lat], "lat", 1)
    south = shift(block[high_lat], "lat", -1)
    west = shift(block[:, low_elev], "elev", 1)
    east = shift(block[:, high_elev], "elev", -1)
    north_west = shift(west[low_lat], "lat", 1)
    north_east = shift(east[low_lat], "lat", 1)
    south_west = shift(west[high_lat], "lat", -1)
    south_east = shift(east[high_lat], "lat", -1)
    center = jnp.concatenate([north, block, south], axis=0)
    left = jnp.concatenate([north_west, west, south_west], axis=0)
    right = jnp.concatenate([north_east, east, south_east], axis=0)
    return left, center, right


def time_matrix(time_taps, frames):
    count_taps = time_taps.shape[0]
    source = jnp.arange(frames, dtype=jnp.int32)[:, None]
    target = jnp.arange(frames, dtype=jnp.int32)[None, :]
    lagged = target - source
    matched = lagged[:, :, None] == jnp.arange(count_taps, dtype=jnp.int32)[None, None, :]
    single = jnp.sum(
        jnp.where(matched, time_taps.astype(jnp.float32)[None, None, :], jnp.float32(0.0)), axis=2
    )
    paired = jnp.kron(jnp.eye(2, dtype=jnp.float32), single)
    return paired.astype(jnp.bfloat16)


def lat_pass(extended, lat_taps, lat_count):
    lat_sum = lat_taps[0] * extended[0:lat_count].astype(jnp.float32)
    for index_tap in range(1, 7):
        lat_sum = lat_sum + lat_taps[index_tap] * extended[
            index_tap : index_tap + lat_count
        ].astype(jnp.float32)
    return lat_sum


def smooth(pieces, lat_taps, elev_taps, lat_count, elev_count):
    left, center, right = pieces
    middle = lat_pass(center, lat_taps, lat_count)
    lat_sum = jnp.concatenate(
        [lat_pass(left, lat_taps, lat_count), middle, lat_pass(right, lat_taps, lat_count)], axis=1
    )
    result = elev_taps[0] * lat_sum[:, 0:elev_count]
    for index_tap in range(1, 7):
        result = result + elev_taps[index_tap] * lat_sum[:, index_tap : index_tap + elev_count]
    return result


def filtered_rows(pieces, lat_taps, elev_taps, matrix, lat_count, elev_count):
    smoothed = smooth(pieces, lat_taps, elev_taps, lat_count, elev_count).astype(jnp.bfloat16)
    flat_rows = smoothed.reshape(-1, matrix.shape[0])
    return jnp.dot(flat_rows, matrix, preferred_element_type=jnp.float32).astype(jnp.bfloat16)


def butterfly_sum(block):
    for axis in ("lat", "elev"):
        count = lax.axis_size(axis)
        stride = 1
        while stride < count:
            pairs = [(i, i ^ stride) for i in range(count)]
            block = block + lax.ppermute(block, axis, pairs)
            stride *= 2
    return block


def packed_gram_sum(gram):
    half = gram.shape[0] // 2
    upper = gram[:half, :half]
    side = gram[:half, half:]
    lower = gram[half:, half:]
    row = jnp.arange(half, dtype=jnp.int32)[:, None]
    col = jnp.arange(half, dtype=jnp.int32)[None, :]
    keep_upper = row <= col
    merged = jnp.where(keep_upper, upper, lower)
    diagonal = jnp.diagonal(lower)[None, :]
    packed = butterfly_sum(jnp.concatenate([side, merged, diagonal], axis=0))
    side = packed[:half]
    merged = packed[half : 2 * half]
    diagonal = packed[2 * half]
    upper = jnp.where(keep_upper, merged, merged.T)
    lower = jnp.where(row > col, merged, merged.T)
    lower = jnp.where(row == col, diagonal[None, :], lower)
    return jnp.concatenate(
        [jnp.concatenate([upper, side], axis=1), jnp.concatenate([side.T, lower], axis=1)], axis=0
    )


def band_filter(gram_sum, clutter_rank, noise_rank, steps=13):
    width = gram_sum.shape[0]
    identity = jnp.eye(width, dtype=jnp.float32)
    total_trace = jnp.sum(gram_sum * identity)
    levels = total_trace / jnp.stack([clutter_rank, noise_rank]).astype(jnp.float32)
    shifted = gram_sum[None] + levels[:, None, None] * identity[None]
    scale = 2.0 / (2.0 * levels + total_trace)
    inverse = scale[:, None, None] * identity[None]

    def refine(_, inverse):
        product = jnp.einsum("bij,bjk->bik", shifted, inverse, precision=lax.Precision.HIGHEST)
        return 2.0 * inverse - jnp.einsum(
            "bij,bjk->bik", inverse, product, precision=lax.Precision.HIGHEST
        )

    inverse = lax.fori_loop(0, steps, refine, inverse)
    resolvents = levels[:, None, None] * inverse
    return resolvents[0] - resolvents[1]


def body(volume, lat_taps, elev_taps, time_taps, clutter_rank, noise_rank):
    lat_count, elev_count, depth, columns = volume.shape
    matrix = time_matrix(time_taps, columns // 2)
    extended = halo_pieces(volume, 3)
    row_block = filtered_rows(extended, lat_taps, elev_taps, matrix, lat_count, elev_count)
    local_gram = lax.dot_general(
        row_block, row_block, (((0,), (0,)), ((), ())), preferred_element_type=jnp.float32
    )
    gram_sum = packed_gram_sum(local_gram)
    weights = band_filter(gram_sum, clutter_rank, noise_rank)
    cleaned_rows = jnp.dot(
        row_block, weights.astype(jnp.bfloat16), preferred_element_type=jnp.float32
    ).astype(jnp.bfloat16)
    cleaned = cleaned_rows.reshape(lat_count, elev_count, depth, columns)
    power = jnp.sum(jnp.square(cleaned.astype(jnp.float32)), axis=3)
    return (cleaned, power, weights)


def solution(mesh):
    placed = (P("lat", "elev", None, None), P(), P(), P(), P(), P())
    return jax.shard_map(
        body,
        mesh=mesh,
        in_specs=placed,
        out_specs=(P("lat", "elev", None, None), P("lat", "elev", None), P()),
        check_vma=False,
    )
```

```python
import jax
import jax.numpy as jnp
from jax import lax
from jax.sharding import PartitionSpec as P


def halo_pieces(block, width):
    lat_size, elev_size = block.shape[0], block.shape[1]
    low_lat = slice(lat_size - width, lat_size)
    high_lat = slice(0, width)
    low_elev = slice(elev_size - width, elev_size)
    high_elev = slice(0, width)

    def shift(piece, axis, step):
        count = lax.axis_size(axis)
        pairs = [(i, i + step) for i in range(count) if 0 <= i + step < count]
        return lax.ppermute(piece, axis, pairs)

    north = shift(block[low_lat], "lat", 1)
    south = shift(block[high_lat], "lat", -1)
    west = shift(block[:, low_elev], "elev", 1)
    east = shift(block[:, high_elev], "elev", -1)
    north_west = shift(west[low_lat], "lat", 1)
    north_east = shift(east[low_lat], "lat", 1)
    south_west = shift(west[high_lat], "lat", -1)
    south_east = shift(east[high_lat], "lat", -1)
    center = jnp.concatenate([north, block, south], axis=0)
    left = jnp.concatenate([north_west, west, south_west], axis=0)
    right = jnp.concatenate([north_east, east, south_east], axis=0)
    return left, center, right


def time_matrix(time_taps, frames):
    count_taps = time_taps.shape[0]
    source = jnp.arange(frames, dtype=jnp.int32)[:, None]
    target = jnp.arange(frames, dtype=jnp.int32)[None, :]
    lagged = target - source
    matched = lagged[:, :, None] == jnp.arange(count_taps, dtype=jnp.int32)[None, None, :]
    single = jnp.sum(
        jnp.where(matched, time_taps.astype(jnp.float32)[None, None, :], jnp.float32(0.0)), axis=2
    )
    paired = jnp.kron(jnp.eye(2, dtype=jnp.float32), single)
    return paired.astype(jnp.bfloat16)


def lat_pass(extended, lat_taps, lat_count):
    lat_sum = lat_taps[0] * extended[0:lat_count].astype(jnp.float32)
    for index_tap in range(1, 7):
        lat_sum = lat_sum + lat_taps[index_tap] * extended[
            index_tap : index_tap + lat_count
        ].astype(jnp.float32)
    return lat_sum


def smooth(pieces, lat_taps, elev_taps, lat_count, elev_count):
    left, center, right = pieces
    middle = lat_pass(center, lat_taps, lat_count)
    lat_sum = jnp.concatenate(
        [lat_pass(left, lat_taps, lat_count), middle, lat_pass(right, lat_taps, lat_count)], axis=1
    )
    result = elev_taps[0] * lat_sum[:, 0:elev_count]
    for index_tap in range(1, 7):
        result = result + elev_taps[index_tap] * lat_sum[:, index_tap : index_tap + elev_count]
    return result


def filtered_rows(pieces, lat_taps, elev_taps, matrix, lat_count, elev_count):
    smoothed = smooth(pieces, lat_taps, elev_taps, lat_count, elev_count).astype(jnp.bfloat16)
    flat_rows = smoothed.reshape(-1, matrix.shape[0])
    return jnp.dot(flat_rows, matrix, preferred_element_type=jnp.float32).astype(jnp.bfloat16)


def butterfly_sum(block, strides):
    for axis, first in strides:
        count = lax.axis_size(axis)
        stride = first
        while stride < count:
            pairs = [(i, i ^ stride) for i in range(count)]
            block = block + lax.ppermute(block, axis, pairs)
            stride *= 2
    return block


def chip_split_sum(block):
    rows = block.shape[0]
    padded_rows = -(-rows // 16) * 16
    block = jnp.pad(block, ((0, padded_rows - rows), (0, 0)))
    swap = [(i, i ^ 1) for i in range(lax.axis_size("lat"))]
    block = block + lax.ppermute(block, "lat", swap)
    half = padded_rows // 2
    core = lax.axis_index("lat") % 2
    own = lax.dynamic_slice_in_dim(block, core * half, half, axis=0)
    own = butterfly_sum(own, (("lat", 2), ("elev", 1)))
    other = lax.ppermute(own, "lat", swap)
    first = jnp.where(core == 0, own, other)
    second = jnp.where(core == 0, other, own)
    return jnp.concatenate([first, second], axis=0)[:rows]


def packed_gram_sum(gram):
    half = gram.shape[0] // 2
    upper = gram[:half, :half]
    side = gram[:half, half:]
    lower = gram[half:, half:]
    row = jnp.arange(half, dtype=jnp.int32)[:, None]
    col = jnp.arange(half, dtype=jnp.int32)[None, :]
    keep_upper = row <= col
    merged = jnp.where(keep_upper, upper, lower)
    diagonal = jnp.diagonal(lower)[None, :]
    packed = chip_split_sum(jnp.concatenate([side, merged, diagonal], axis=0))
    side = packed[:half]
    merged = packed[half : 2 * half]
    diagonal = packed[2 * half]
    upper = jnp.where(keep_upper, merged, merged.T)
    lower = jnp.where(row > col, merged, merged.T)
    lower = jnp.where(row == col, diagonal[None, :], lower)
    return jnp.concatenate(
        [jnp.concatenate([upper, side], axis=1), jnp.concatenate([side.T, lower], axis=1)], axis=0
    )


def band_filter(gram_sum, clutter_rank, noise_rank, steps=9):
    width = gram_sum.shape[0]
    identity = jnp.eye(width, dtype=jnp.float32)
    total_trace = jnp.sum(gram_sum * identity)
    levels = total_trace / jnp.stack([clutter_rank, noise_rank]).astype(jnp.float32)
    shifted = gram_sum[None] + levels[:, None, None] * identity[None]
    scale = 2.0 / (2.0 * levels + total_trace)
    inverse = scale[:, None, None] * identity[None]
    low = scale * levels

    def refine(_, carry):
        inverse, low = carry
        squeezed = low * (2.0 - low)
        factor = 2.0 / (1.0 + squeezed)
        product = jnp.einsum("bij,bjk->bik", shifted, inverse, precision=lax.Precision.HIGHEST)
        inverse = factor[:, None, None] * (
            2.0 * inverse
            - jnp.einsum("bij,bjk->bik", inverse, product, precision=lax.Precision.HIGHEST)
        )
        return inverse, factor * squeezed

    inverse, _ = lax.fori_loop(0, steps, refine, (inverse, low))
    resolvents = levels[:, None, None] * inverse
    return resolvents[0] - resolvents[1]


def body(volume, lat_taps, elev_taps, time_taps, clutter_rank, noise_rank):
    lat_count, elev_count, depth, columns = volume.shape
    matrix = time_matrix(time_taps, columns // 2)
    extended = halo_pieces(volume, 3)
    row_block = filtered_rows(extended, lat_taps, elev_taps, matrix, lat_count, elev_count)
    local_gram = lax.dot_general(
        row_block, row_block, (((0,), (0,)), ((), ())), preferred_element_type=jnp.float32
    )
    gram_sum = packed_gram_sum(local_gram)
    weights = band_filter(gram_sum, clutter_rank, noise_rank)
    cleaned_rows = jnp.dot(
        row_block, weights.astype(jnp.bfloat16), preferred_element_type=jnp.float32
    ).astype(jnp.bfloat16)
    cleaned = cleaned_rows.reshape(lat_count, elev_count, depth, columns)
    power = jnp.sum(jnp.square(cleaned.astype(jnp.float32)), axis=3)
    return (cleaned, power, weights)


def solution(mesh):
    placed = (P("lat", "elev", None, None), P(), P(), P(), P(), P())
    return jax.shard_map(
        body,
        mesh=mesh,
        in_specs=placed,
        out_specs=(P("lat", "elev", None, None), P("lat", "elev", None), P()),
        check_vma=False,
    )
```

```python
import jax
import jax.numpy as jnp
from jax import lax
from jax.sharding import PartitionSpec as P


def halo_pieces(block, width):
    lat_size, elev_size = block.shape[0], block.shape[1]
    low_lat = slice(lat_size - width, lat_size)
    high_lat = slice(0, width)
    low_elev = slice(elev_size - width, elev_size)
    high_elev = slice(0, width)

    def shift(piece, axis, step):
        count = lax.axis_size(axis)
        pairs = [(i, i + step) for i in range(count) if 0 <= i + step < count]
        return lax.ppermute(piece, axis, pairs)

    north = shift(block[low_lat], "lat", 1)
    south = shift(block[high_lat], "lat", -1)
    west = shift(block[:, low_elev], "elev", 1)
    east = shift(block[:, high_elev], "elev", -1)
    north_west = shift(west[low_lat], "lat", 1)
    north_east = shift(east[low_lat], "lat", 1)
    south_west = shift(west[high_lat], "lat", -1)
    south_east = shift(east[high_lat], "lat", -1)
    center = jnp.concatenate([north, block, south], axis=0)
    left = jnp.concatenate([north_west, west, south_west], axis=0)
    right = jnp.concatenate([north_east, east, south_east], axis=0)
    return left, center, right


def time_matrix(time_taps, frames):
    count_taps = time_taps.shape[0]
    source = jnp.arange(frames, dtype=jnp.int32)[:, None]
    target = jnp.arange(frames, dtype=jnp.int32)[None, :]
    lagged = target - source
    matched = lagged[:, :, None] == jnp.arange(count_taps, dtype=jnp.int32)[None, None, :]
    single = jnp.sum(
        jnp.where(matched, time_taps.astype(jnp.float32)[None, None, :], jnp.float32(0.0)), axis=2
    )
    paired = jnp.kron(jnp.eye(2, dtype=jnp.float32), single)
    return paired.astype(jnp.bfloat16)


def lat_pass(extended, lat_taps, lat_count):
    lat_sum = lat_taps[0] * extended[0:lat_count].astype(jnp.float32)
    for index_tap in range(1, 7):
        lat_sum = lat_sum + lat_taps[index_tap] * extended[
            index_tap : index_tap + lat_count
        ].astype(jnp.float32)
    return lat_sum


def smooth(pieces, lat_taps, elev_taps, lat_count, elev_count):
    left, center, right = pieces
    middle = lat_pass(center, lat_taps, lat_count)
    lat_sum = jnp.concatenate(
        [lat_pass(left, lat_taps, lat_count), middle, lat_pass(right, lat_taps, lat_count)], axis=1
    )
    result = elev_taps[0] * lat_sum[:, 0:elev_count]
    for index_tap in range(1, 7):
        result = result + elev_taps[index_tap] * lat_sum[:, index_tap : index_tap + elev_count]
    return result


def filtered_rows(pieces, lat_taps, elev_taps, matrix, lat_count, elev_count):
    smoothed = smooth(pieces, lat_taps, elev_taps, lat_count, elev_count).astype(jnp.bfloat16)
    flat_rows = smoothed.reshape(-1, matrix.shape[0])
    return jnp.dot(flat_rows, matrix, preferred_element_type=jnp.float32).astype(jnp.bfloat16)


def butterfly_sum(block, groups):
    for axis, strides in groups:
        count = lax.axis_size(axis)
        received = []
        for mask in strides:
            if mask < count:
                received.append(lax.ppermute(block, axis, [(i, i ^ mask) for i in range(count)]))
        if len(received) == 3:
            block = (block + received[0]) + (received[1] + received[2])
        elif received:
            block = block + received[0]
    return block


def radix_groups(axis, first):
    count = lax.axis_size(axis)
    groups = []
    stride = first
    while stride < count:
        if 2 * stride < count:
            groups.append((axis, (stride, 2 * stride, 3 * stride)))
            stride *= 4
        else:
            groups.append((axis, (stride,)))
            stride *= 2
    return groups


def chip_split_sum(block):
    rows = block.shape[0]
    padded_rows = -(-rows // 16) * 16
    block = jnp.pad(block, ((0, padded_rows - rows), (0, 0)))
    swap = [(i, i ^ 1) for i in range(lax.axis_size("lat"))]
    block = block + lax.ppermute(block, "lat", swap)
    half = padded_rows // 2
    core = lax.axis_index("lat") % 2
    own = lax.dynamic_slice_in_dim(block, core * half, half, axis=0)
    own = butterfly_sum(own, radix_groups("lat", 2) + radix_groups("elev", 1))
    other = lax.ppermute(own, "lat", swap)
    first = jnp.where(core == 0, own, other)
    second = jnp.where(core == 0, other, own)
    return jnp.concatenate([first, second], axis=0)[:rows]


def packed_gram_sum(gram):
    half = gram.shape[0] // 2
    upper = gram[:half, :half]
    side = gram[:half, half:]
    lower = gram[half:, half:]
    row = jnp.arange(half, dtype=jnp.int32)[:, None]
    col = jnp.arange(half, dtype=jnp.int32)[None, :]
    keep_upper = row <= col
    merged = jnp.where(keep_upper, upper, lower)
    diagonal = jnp.diagonal(lower)[None, :]
    packed = chip_split_sum(jnp.concatenate([side, merged, diagonal], axis=0))
    side = packed[:half]
    merged = packed[half : 2 * half]
    diagonal = packed[2 * half]
    upper = jnp.where(keep_upper, merged, merged.T)
    lower = jnp.where(row > col, merged, merged.T)
    lower = jnp.where(row == col, diagonal[None, :], lower)
    return jnp.concatenate(
        [jnp.concatenate([upper, side], axis=1), jnp.concatenate([side.T, lower], axis=1)], axis=0
    )


def band_filter(gram_sum, clutter_rank, noise_rank, steps=9):
    width = gram_sum.shape[0]
    identity = jnp.eye(width, dtype=jnp.float32)
    total_trace = jnp.sum(gram_sum * identity)
    levels = total_trace / jnp.stack([clutter_rank, noise_rank]).astype(jnp.float32)
    shifted = gram_sum[None] + levels[:, None, None] * identity[None]
    scale = 2.0 / (2.0 * levels + total_trace)
    inverse = scale[:, None, None] * identity[None]
    low = scale * levels

    def refine(_, carry):
        inverse, low = carry
        squeezed = low * (2.0 - low)
        factor = 2.0 / (1.0 + squeezed)
        product = jnp.einsum("bij,bjk->bik", shifted, inverse, precision=lax.Precision.HIGHEST)
        inverse = factor[:, None, None] * (
            2.0 * inverse
            - jnp.einsum("bij,bjk->bik", inverse, product, precision=lax.Precision.HIGHEST)
        )
        return inverse, factor * squeezed

    inverse, _ = lax.fori_loop(0, steps, refine, (inverse, low))
    resolvents = levels[:, None, None] * inverse
    return resolvents[0] - resolvents[1]


def body(volume, lat_taps, elev_taps, time_taps, clutter_rank, noise_rank):
    lat_count, elev_count, depth, columns = volume.shape
    matrix = time_matrix(time_taps, columns // 2)
    extended = halo_pieces(volume, 3)
    row_block = filtered_rows(extended, lat_taps, elev_taps, matrix, lat_count, elev_count)
    local_gram = lax.dot_general(
        row_block, row_block, (((0,), (0,)), ((), ())), preferred_element_type=jnp.float32
    )
    gram_sum = packed_gram_sum(local_gram)
    weights = band_filter(gram_sum, clutter_rank, noise_rank)
    cleaned_rows = jnp.dot(
        row_block, weights.astype(jnp.bfloat16), preferred_element_type=jnp.float32
    ).astype(jnp.bfloat16)
    cleaned = cleaned_rows.reshape(lat_count, elev_count, depth, columns)
    power = jnp.sum(jnp.square(cleaned.astype(jnp.float32)), axis=3)
    return (cleaned, power, weights)


def solution(mesh):
    placed = (P("lat", "elev", None, None), P(), P(), P(), P(), P())
    return jax.shard_map(
        body,
        mesh=mesh,
        in_specs=placed,
        out_specs=(P("lat", "elev", None, None), P("lat", "elev", None), P()),
        check_vma=False,
    )
```

```python
import jax
import jax.numpy as jnp
from jax import lax
from jax.experimental import pallas as pl
from jax.experimental.pallas import tpu as pltpu
from jax.sharding import PartitionSpec as P


def halo_pieces(block, width):
    lat_size, elev_size = block.shape[0], block.shape[1]
    low_lat = slice(lat_size - width, lat_size)
    high_lat = slice(0, width)
    low_elev = slice(elev_size - width, elev_size)
    high_elev = slice(0, width)

    def shift(piece, axis, step):
        count = lax.axis_size(axis)
        pairs = [(i, i + step) for i in range(count) if 0 <= i + step < count]
        return lax.ppermute(piece, axis, pairs)

    north = shift(block[low_lat], "lat", 1)
    south = shift(block[high_lat], "lat", -1)
    west = shift(block[:, low_elev], "elev", 1)
    east = shift(block[:, high_elev], "elev", -1)
    north_west = shift(west[low_lat], "lat", 1)
    north_east = shift(east[low_lat], "lat", 1)
    south_west = shift(west[high_lat], "lat", -1)
    south_east = shift(east[high_lat], "lat", -1)
    center = jnp.concatenate([north, block, south], axis=0)
    left = jnp.concatenate([north_west, west, south_west], axis=0)
    right = jnp.concatenate([north_east, east, south_east], axis=0)
    return left, center, right


def time_matrix(time_taps, frames):
    count_taps = time_taps.shape[0]
    source = jnp.arange(frames, dtype=jnp.int32)[:, None]
    target = jnp.arange(frames, dtype=jnp.int32)[None, :]
    lagged = target - source
    matched = lagged[:, :, None] == jnp.arange(count_taps, dtype=jnp.int32)[None, None, :]
    single = jnp.sum(
        jnp.where(matched, time_taps.astype(jnp.float32)[None, None, :], jnp.float32(0.0)), axis=2
    )
    paired = jnp.kron(jnp.eye(2, dtype=jnp.float32), single)
    return paired.astype(jnp.bfloat16)


def lat_pass(extended, lat_taps, lat_count):
    lat_sum = lat_taps[0] * extended[0:lat_count].astype(jnp.float32)
    for index_tap in range(1, 7):
        lat_sum = lat_sum + lat_taps[index_tap] * extended[
            index_tap : index_tap + lat_count
        ].astype(jnp.float32)
    return lat_sum


def edge_smooth_kernel(lat_ref, elev_ref, middle_ref, left_ref, right_ref, out_ref):
    lat_taps = [lat_ref[i] for i in range(7)]
    elev_taps = [elev_ref[i] for i in range(7)]
    lat_count, elev_count = out_ref.shape[0], out_ref.shape[1]

    def side_rows(side_ref):
        rows = [side_ref[k].astype(jnp.float32) for k in range(side_ref.shape[0])]
        sums = []
        for l in range(lat_count):
            total = lat_taps[0] * rows[l]
            for i in range(1, 7):
                total = total + lat_taps[i] * rows[l + i]
            sums.append(total)
        return sums

    left = side_rows(left_ref)
    right = side_rows(right_ref)
    width = left_ref.shape[1]
    for l in range(lat_count):
        columns = [left[l][k] for k in range(width)]
        columns += [middle_ref[l, k] for k in range(elev_count)]
        columns += [right[l][k] for k in range(width)]
        for e in range(elev_count):
            total = elev_taps[0] * columns[e]
            for j in range(1, 7):
                total = total + elev_taps[j] * columns[e + j]
            out_ref[l, e] = total.astype(out_ref.dtype)


def edge_smooth(middle, left, right, lat_taps, elev_taps, tile=16):
    lat_count, elev_count, depth, columns = middle.shape
    tile = tile if depth % tile == 0 else depth
    rows, width = left.shape[0], left.shape[1]
    smem = pl.BlockSpec(memory_space=pltpu.SMEM)
    return pl.pallas_call(
        edge_smooth_kernel,
        out_shape=jax.ShapeDtypeStruct(middle.shape, jnp.bfloat16),
        grid=(depth // tile,),
        in_specs=[
            smem,
            smem,
            pl.BlockSpec((lat_count, elev_count, tile, columns), lambda k: (0, 0, k, 0)),
            pl.BlockSpec((rows, width, tile, columns), lambda k: (0, 0, k, 0)),
            pl.BlockSpec((rows, width, tile, columns), lambda k: (0, 0, k, 0)),
        ],
        out_specs=pl.BlockSpec((lat_count, elev_count, tile, columns), lambda k: (0, 0, k, 0)),
        interpret=INTERPRET,
    )(lat_taps, elev_taps, middle, left, right)


INTERPRET = False


def smooth(pieces, lat_taps, elev_taps, lat_count):
    left, center, right = pieces
    middle = lat_pass(center, lat_taps, lat_count)
    return edge_smooth(middle, left, right, lat_taps, elev_taps)


def filtered_rows(pieces, lat_taps, elev_taps, matrix, lat_count):
    smoothed = smooth(pieces, lat_taps, elev_taps, lat_count)
    flat_rows = smoothed.reshape(-1, matrix.shape[0])
    return jnp.dot(flat_rows, matrix, preferred_element_type=jnp.float32).astype(jnp.bfloat16)


def butterfly_sum(block, groups):
    for axis, strides in groups:
        count = lax.axis_size(axis)
        received = []
        for mask in strides:
            if mask < count:
                received.append(lax.ppermute(block, axis, [(i, i ^ mask) for i in range(count)]))
        if len(received) == 3:
            block = (block + received[0]) + (received[1] + received[2])
        elif received:
            block = block + received[0]
    return block


def radix_groups(axis, first):
    count = lax.axis_size(axis)
    groups = []
    stride = first
    while stride < count:
        if 2 * stride < count:
            groups.append((axis, (stride, 2 * stride, 3 * stride)))
            stride *= 4
        else:
            groups.append((axis, (stride,)))
            stride *= 2
    return groups


def chip_split_sum(block):
    rows = block.shape[0]
    padded_rows = -(-rows // 16) * 16
    block = jnp.pad(block, ((0, padded_rows - rows), (0, 0)))
    swap = [(i, i ^ 1) for i in range(lax.axis_size("lat"))]
    block = block + lax.ppermute(block, "lat", swap)
    half = padded_rows // 2
    core = lax.axis_index("lat") % 2
    own = lax.dynamic_slice_in_dim(block, core * half, half, axis=0)
    own = butterfly_sum(own, radix_groups("lat", 2) + radix_groups("elev", 1))
    other = lax.ppermute(own, "lat", swap)
    first = jnp.where(core == 0, own, other)
    second = jnp.where(core == 0, other, own)
    return jnp.concatenate([first, second], axis=0)[:rows]


def packed_gram_sum(gram):
    half = gram.shape[0] // 2
    upper = gram[:half, :half]
    side = gram[:half, half:]
    lower = gram[half:, half:]
    row = jnp.arange(half, dtype=jnp.int32)[:, None]
    col = jnp.arange(half, dtype=jnp.int32)[None, :]
    keep_upper = row <= col
    merged = jnp.where(keep_upper, upper, lower)
    diagonal = jnp.diagonal(lower)[None, :]
    packed = chip_split_sum(jnp.concatenate([side, merged, diagonal], axis=0))
    side = packed[:half]
    merged = packed[half : 2 * half]
    diagonal = packed[2 * half]
    upper = jnp.where(keep_upper, merged, merged.T)
    lower = jnp.where(row > col, merged, merged.T)
    lower = jnp.where(row == col, diagonal[None, :], lower)
    return jnp.concatenate(
        [jnp.concatenate([upper, side], axis=1), jnp.concatenate([side.T, lower], axis=1)], axis=0
    )


def band_filter(gram_sum, clutter_rank, noise_rank, steps=9):
    width = gram_sum.shape[0]
    identity = jnp.eye(width, dtype=jnp.float32)
    total_trace = jnp.sum(gram_sum * identity)
    levels = total_trace / jnp.stack([clutter_rank, noise_rank]).astype(jnp.float32)
    shifted = gram_sum[None] + levels[:, None, None] * identity[None]
    scale = 2.0 / (2.0 * levels + total_trace)
    inverse = scale[:, None, None] * identity[None]
    low = scale * levels

    def refine(_, carry):
        inverse, low = carry
        squeezed = low * (2.0 - low)
        factor = 2.0 / (1.0 + squeezed)
        product = jnp.einsum("bij,bjk->bik", shifted, inverse, precision=lax.Precision.HIGHEST)
        inverse = factor[:, None, None] * (
            2.0 * inverse
            - jnp.einsum("bij,bjk->bik", inverse, product, precision=lax.Precision.HIGHEST)
        )
        return inverse, factor * squeezed

    inverse, _ = lax.fori_loop(0, steps, refine, (inverse, low))
    resolvents = levels[:, None, None] * inverse
    return resolvents[0] - resolvents[1]


def body(volume, lat_taps, elev_taps, time_taps, clutter_rank, noise_rank):
    lat_count, elev_count, depth, columns = volume.shape
    matrix = time_matrix(time_taps, columns // 2)
    extended = halo_pieces(volume, 3)
    row_block = filtered_rows(extended, lat_taps, elev_taps, matrix, lat_count)
    local_gram = lax.dot_general(
        row_block, row_block, (((0,), (0,)), ((), ())), preferred_element_type=jnp.float32
    )
    gram_sum = packed_gram_sum(local_gram)
    weights = band_filter(gram_sum, clutter_rank, noise_rank)
    cleaned_rows = jnp.dot(
        row_block, weights.astype(jnp.bfloat16), preferred_element_type=jnp.float32
    ).astype(jnp.bfloat16)
    cleaned = cleaned_rows.reshape(lat_count, elev_count, depth, columns)
    power = jnp.sum(jnp.square(cleaned.astype(jnp.float32)), axis=3)
    return (cleaned, power, weights)


def solution(mesh):
    placed = (P("lat", "elev", None, None), P(), P(), P(), P(), P())
    return jax.shard_map(
        body,
        mesh=mesh,
        in_specs=placed,
        out_specs=(P("lat", "elev", None, None), P("lat", "elev", None), P()),
        check_vma=False,
    )
```

```python
import jax
import jax.numpy as jnp
from jax import lax
from jax.experimental import pallas as pl
from jax.experimental.pallas import tpu as pltpu
from jax.sharding import PartitionSpec as P


def halo_pieces(block, width):
    lat_size, elev_size = block.shape[0], block.shape[1]
    low_lat = slice(lat_size - width, lat_size)
    high_lat = slice(0, width)
    low_elev = slice(elev_size - width, elev_size)
    high_elev = slice(0, width)

    def shift(piece, axis, step):
        count = lax.axis_size(axis)
        pairs = [(i, i + step) for i in range(count) if 0 <= i + step < count]
        return lax.ppermute(piece, axis, pairs)

    north = shift(block[low_lat], "lat", 1)
    south = shift(block[high_lat], "lat", -1)
    west = shift(block[:, low_elev], "elev", 1)
    east = shift(block[:, high_elev], "elev", -1)
    north_west = shift(west[low_lat], "lat", 1)
    north_east = shift(east[low_lat], "lat", 1)
    south_west = shift(west[high_lat], "lat", -1)
    south_east = shift(east[high_lat], "lat", -1)
    center = jnp.concatenate([north, block, south], axis=0)
    left = (north_west, west, south_west)
    right = (north_east, east, south_east)
    return left, center, right


def time_matrix(time_taps, frames):
    count_taps = time_taps.shape[0]
    source = jnp.arange(frames, dtype=jnp.int32)[:, None]
    target = jnp.arange(frames, dtype=jnp.int32)[None, :]
    lagged = target - source
    matched = lagged[:, :, None] == jnp.arange(count_taps, dtype=jnp.int32)[None, None, :]
    single = jnp.sum(
        jnp.where(matched, time_taps.astype(jnp.float32)[None, None, :], jnp.float32(0.0)), axis=2
    )
    paired = jnp.kron(jnp.eye(2, dtype=jnp.float32), single)
    return paired.astype(jnp.bfloat16)


def lat_pass(extended, lat_taps, lat_count):
    lat_sum = lat_taps[0] * extended[0:lat_count].astype(jnp.float32)
    for index_tap in range(1, 7):
        lat_sum = lat_sum + lat_taps[index_tap] * extended[
            index_tap : index_tap + lat_count
        ].astype(jnp.float32)
    return lat_sum


def edge_smooth_kernel(lat_ref, elev_ref, middle_ref, *refs):
    out_ref = refs[-1]
    left_refs, right_refs = refs[0:3], refs[3:6]
    lat_taps = [lat_ref[i] for i in range(7)]
    elev_taps = [elev_ref[i] for i in range(7)]
    lat_count, elev_count = out_ref.shape[0], out_ref.shape[1]

    def side_rows(side_refs):
        rows = [ref[k].astype(jnp.float32) for ref in side_refs for k in range(ref.shape[0])]
        sums = []
        for l in range(lat_count):
            total = lat_taps[0] * rows[l]
            for i in range(1, 7):
                total = total + lat_taps[i] * rows[l + i]
            sums.append(total)
        return sums

    left = side_rows(left_refs)
    right = side_rows(right_refs)
    width = left_refs[0].shape[1]
    for l in range(lat_count):
        columns = [left[l][k] for k in range(width)]
        columns += [middle_ref[l, k] for k in range(elev_count)]
        columns += [right[l][k] for k in range(width)]
        for e in range(elev_count):
            total = elev_taps[0] * columns[e]
            for j in range(1, 7):
                total = total + elev_taps[j] * columns[e + j]
            out_ref[l, e] = total.astype(out_ref.dtype)


def edge_smooth(middle, left, right, lat_taps, elev_taps, tile=16):
    _, _, depth, columns = middle.shape
    tile = tile if depth % tile == 0 else depth
    smem = pl.BlockSpec(memory_space=pltpu.SMEM)

    def tiled(piece):
        return pl.BlockSpec((piece.shape[0], piece.shape[1], tile, columns), lambda k: (0, 0, k, 0))

    sides = (*left, *right)
    return pl.pallas_call(
        edge_smooth_kernel,
        out_shape=jax.ShapeDtypeStruct(middle.shape, jnp.bfloat16),
        grid=(depth // tile,),
        in_specs=[smem, smem, tiled(middle), *[tiled(piece) for piece in sides]],
        out_specs=tiled(middle),
        interpret=INTERPRET,
    )(lat_taps, elev_taps, middle, *sides)


INTERPRET = False


def smooth(pieces, lat_taps, elev_taps, lat_count):
    left, center, right = pieces
    middle = lat_pass(center, lat_taps, lat_count)
    return edge_smooth(middle, left, right, lat_taps, elev_taps)


def filtered_rows(pieces, lat_taps, elev_taps, matrix, lat_count):
    smoothed = smooth(pieces, lat_taps, elev_taps, lat_count)
    flat_rows = smoothed.reshape(-1, matrix.shape[0])
    return jnp.dot(flat_rows, matrix, preferred_element_type=jnp.float32).astype(jnp.bfloat16)


def butterfly_sum(block, groups):
    for axis, strides in groups:
        count = lax.axis_size(axis)
        received = []
        for mask in strides:
            if mask < count:
                received.append(lax.ppermute(block, axis, [(i, i ^ mask) for i in range(count)]))
        if len(received) == 3:
            block = (block + received[0]) + (received[1] + received[2])
        elif received:
            block = block + received[0]
    return block


def radix_groups(axis, first):
    count = lax.axis_size(axis)
    groups = []
    stride = first
    while stride < count:
        if 2 * stride < count:
            groups.append((axis, (stride, 2 * stride, 3 * stride)))
            stride *= 4
        else:
            groups.append((axis, (stride,)))
            stride *= 2
    return groups


def chip_split_sum(block):
    rows = block.shape[0]
    padded_rows = -(-rows // 16) * 16
    block = jnp.pad(block, ((0, padded_rows - rows), (0, 0)))
    swap = [(i, i ^ 1) for i in range(lax.axis_size("lat"))]
    block = block + lax.ppermute(block, "lat", swap)
    half = padded_rows // 2
    core = lax.axis_index("lat") % 2
    own = lax.dynamic_slice_in_dim(block, core * half, half, axis=0)
    own = butterfly_sum(own, radix_groups("lat", 2) + radix_groups("elev", 1))
    other = lax.ppermute(own, "lat", swap)
    first = jnp.where(core == 0, own, other)
    second = jnp.where(core == 0, other, own)
    return jnp.concatenate([first, second], axis=0)[:rows]


def packed_gram_sum(gram):
    half = gram.shape[0] // 2
    upper = gram[:half, :half]
    side = gram[:half, half:]
    lower = gram[half:, half:]
    row = jnp.arange(half, dtype=jnp.int32)[:, None]
    col = jnp.arange(half, dtype=jnp.int32)[None, :]
    keep_upper = row <= col
    merged = jnp.where(keep_upper, upper, lower)
    diagonal = jnp.diagonal(lower)[None, :]
    packed = chip_split_sum(jnp.concatenate([side, merged, diagonal], axis=0))
    side = packed[:half]
    merged = packed[half : 2 * half]
    diagonal = packed[2 * half]
    upper = jnp.where(keep_upper, merged, merged.T)
    lower = jnp.where(row > col, merged, merged.T)
    lower = jnp.where(row == col, diagonal[None, :], lower)
    return jnp.concatenate(
        [jnp.concatenate([upper, side], axis=1), jnp.concatenate([side.T, lower], axis=1)], axis=0
    )


def band_filter(gram_sum, clutter_rank, noise_rank, steps=9, coarse_steps=5):
    width = gram_sum.shape[0]
    identity = jnp.eye(width, dtype=jnp.float32)
    total_trace = jnp.sum(gram_sum * identity)
    levels = total_trace / jnp.stack([clutter_rank, noise_rank]).astype(jnp.float32)
    shifted = gram_sum[None] + levels[:, None, None] * identity[None]
    scale = 2.0 / (2.0 * levels + total_trace)
    inverse = scale[:, None, None] * identity[None]
    low = scale * levels

    def refine(precision):
        def step(_, carry):
            inverse, low = carry
            squeezed = low * (2.0 - low)
            factor = 2.0 / (1.0 + squeezed)
            product = jnp.einsum("bij,bjk->bik", shifted, inverse, precision=precision)
            inverse = factor[:, None, None] * (
                2.0 * inverse - jnp.einsum("bij,bjk->bik", inverse, product, precision=precision)
            )
            return inverse, factor * squeezed

        return step

    carry = lax.fori_loop(0, coarse_steps, refine(lax.Precision.HIGH), (inverse, low))
    inverse, _ = lax.fori_loop(coarse_steps, steps, refine(lax.Precision.HIGHEST), carry)
    resolvents = levels[:, None, None] * inverse
    return resolvents[0] - resolvents[1]


def body(volume, lat_taps, elev_taps, time_taps, clutter_rank, noise_rank):
    lat_count, elev_count, depth, columns = volume.shape
    matrix = time_matrix(time_taps, columns // 2)
    extended = halo_pieces(volume, 3)
    row_block = filtered_rows(extended, lat_taps, elev_taps, matrix, lat_count)
    local_gram = lax.dot_general(
        row_block, row_block, (((0,), (0,)), ((), ())), preferred_element_type=jnp.float32
    )
    gram_sum = packed_gram_sum(local_gram)
    weights = band_filter(gram_sum, clutter_rank, noise_rank)
    cleaned_rows = jnp.dot(
        row_block, weights.astype(jnp.bfloat16), preferred_element_type=jnp.float32
    ).astype(jnp.bfloat16)
    cleaned = cleaned_rows.reshape(lat_count, elev_count, depth, columns)
    power = jnp.sum(jnp.square(cleaned.astype(jnp.float32)), axis=3)
    return (cleaned, power, weights)


def solution(mesh):
    placed = (P("lat", "elev", None, None), P(), P(), P(), P(), P())
    return jax.shard_map(
        body,
        mesh=mesh,
        in_specs=placed,
        out_specs=(P("lat", "elev", None, None), P("lat", "elev", None), P()),
        check_vma=False,
    )
```

```python
import jax
import jax.numpy as jnp
from jax import lax
from jax.experimental import pallas as pl
from jax.experimental.pallas import tpu as pltpu
from jax.sharding import PartitionSpec as P


def halo_pieces(block, width):
    lat_size, elev_size = block.shape[0], block.shape[1]
    low_lat = slice(lat_size - width, lat_size)
    high_lat = slice(0, width)
    low_elev = slice(elev_size - width, elev_size)
    high_elev = slice(0, width)

    def shift(piece, axis, step):
        count = lax.axis_size(axis)
        pairs = [(i, i + step) for i in range(count) if 0 <= i + step < count]
        return lax.ppermute(piece, axis, pairs)

    north = shift(block[low_lat], "lat", 1)
    south = shift(block[high_lat], "lat", -1)
    west = shift(block[:, low_elev], "elev", 1)
    east = shift(block[:, high_elev], "elev", -1)
    north_west = shift(west[low_lat], "lat", 1)
    north_east = shift(east[low_lat], "lat", 1)
    south_west = shift(west[high_lat], "lat", -1)
    south_east = shift(east[high_lat], "lat", -1)
    center = (block, north, south)
    left = (north_west, west, south_west)
    right = (north_east, east, south_east)
    return left, center, right


def time_matrix(time_taps, frames):
    count_taps = time_taps.shape[0]
    source = jnp.arange(frames, dtype=jnp.int32)[:, None]
    target = jnp.arange(frames, dtype=jnp.int32)[None, :]
    lagged = target - source
    matched = lagged[:, :, None] == jnp.arange(count_taps, dtype=jnp.int32)[None, None, :]
    single = jnp.sum(
        jnp.where(matched, time_taps.astype(jnp.float32)[None, None, :], jnp.float32(0.0)), axis=2
    )
    paired = jnp.kron(jnp.eye(2, dtype=jnp.float32), single)
    return paired.astype(jnp.bfloat16)


def lat_rows(rows, lat_taps, lat_count):
    sums = []
    for l in range(lat_count):
        total = lat_taps[0] * rows[l]
        for i in range(1, 7):
            total = total + lat_taps[i] * rows[l + i]
        sums.append(total)
    return sums


def center_smooth_kernel(lat_ref, elev_ref, block_ref, north_ref, south_ref, out_ref):
    lat_taps = [lat_ref[i] for i in range(7)]
    elev_taps = [elev_ref[i] for i in range(7)]
    lat_count, elev_count = out_ref.shape[0], out_ref.shape[1]
    refs = (north_ref, block_ref, south_ref)
    rows = [ref[k].astype(jnp.float32) for ref in refs for k in range(ref.shape[0])]
    for l, row in enumerate(lat_rows(rows, lat_taps, lat_count)):
        for e in range(elev_count):
            taps = [j for j in range(7) if 0 <= e + j - 3 < elev_count]
            total = elev_taps[taps[0]] * row[e + taps[0] - 3]
            for j in taps[1:]:
                total = total + elev_taps[j] * row[e + j - 3]
            out_ref[l, e] = total


def edge_smooth_kernel(lat_ref, elev_ref, middle_ref, *refs):
    out_ref = refs[-1]
    left_refs, right_refs = refs[0:3], refs[3:6]
    lat_taps = [lat_ref[i] for i in range(7)]
    elev_taps = [elev_ref[i] for i in range(7)]
    lat_count, elev_count = out_ref.shape[0], out_ref.shape[1]
    width = left_refs[0].shape[1]

    def side_rows(side_refs):
        rows = [ref[k].astype(jnp.float32) for ref in side_refs for k in range(ref.shape[0])]
        return lat_rows(rows, lat_taps, lat_count)

    left = side_rows(left_refs)
    right = side_rows(right_refs)
    for l in range(lat_count):
        for e in range(elev_count):
            total = middle_ref[l, e]
            for j in range(7):
                column = e + j
                if column < width:
                    total = total + elev_taps[j] * left[l][column]
                elif column >= width + elev_count:
                    total = total + elev_taps[j] * right[l][column - width - elev_count]
            out_ref[l, e] = total.astype(out_ref.dtype)


def tiled_call(kernel, pieces, out_dtype, lat_taps, elev_taps, tile=16):
    _, _, depth, columns = pieces[0].shape
    tile = tile if depth % tile == 0 else depth
    smem = pl.BlockSpec(memory_space=pltpu.SMEM)

    def tiled(piece):
        return pl.BlockSpec((piece.shape[0], piece.shape[1], tile, columns), lambda k: (0, 0, k, 0))

    return pl.pallas_call(
        kernel,
        out_shape=jax.ShapeDtypeStruct(pieces[0].shape, out_dtype),
        grid=(depth // tile,),
        in_specs=[smem, smem, *[tiled(piece) for piece in pieces]],
        out_specs=tiled(pieces[0]),
        interpret=INTERPRET,
    )(lat_taps, elev_taps, *pieces)


INTERPRET = False


def smooth(pieces, lat_taps, elev_taps):
    left, center, right = pieces
    middle = tiled_call(center_smooth_kernel, center, jnp.float32, lat_taps, elev_taps)
    return tiled_call(edge_smooth_kernel, (middle, *left, *right), jnp.bfloat16, lat_taps, elev_taps)


def filtered_rows(pieces, lat_taps, elev_taps, matrix):
    smoothed = smooth(pieces, lat_taps, elev_taps)
    flat_rows = smoothed.reshape(-1, matrix.shape[0])
    return jnp.dot(flat_rows, matrix, preferred_element_type=jnp.float32).astype(jnp.bfloat16)


def butterfly_sum(block, groups):
    for axis, strides in groups:
        count = lax.axis_size(axis)
        received = []
        for mask in strides:
            if mask < count:
                received.append(lax.ppermute(block, axis, [(i, i ^ mask) for i in range(count)]))
        if len(received) == 3:
            block = (block + received[0]) + (received[1] + received[2])
        elif received:
            block = block + received[0]
    return block


def radix_groups(axis, first):
    count = lax.axis_size(axis)
    groups = []
    stride = first
    while stride < count:
        if 2 * stride < count:
            groups.append((axis, (stride, 2 * stride, 3 * stride)))
            stride *= 4
        else:
            groups.append((axis, (stride,)))
            stride *= 2
    return groups


def chip_split_sum(block):
    rows = block.shape[0]
    padded_rows = -(-rows // 16) * 16
    block = jnp.pad(block, ((0, padded_rows - rows), (0, 0)))
    swap = [(i, i ^ 1) for i in range(lax.axis_size("lat"))]
    block = block + lax.ppermute(block, "lat", swap)
    half = padded_rows // 2
    core = lax.axis_index("lat") % 2
    own = lax.dynamic_slice_in_dim(block, core * half, half, axis=0)
    own = butterfly_sum(own, radix_groups("lat", 2) + radix_groups("elev", 1))
    other = lax.ppermute(own, "lat", swap)
    first = jnp.where(core == 0, own, other)
    second = jnp.where(core == 0, other, own)
    return jnp.concatenate([first, second], axis=0)[:rows]


def packed_gram_sum(gram):
    half = gram.shape[0] // 2
    upper = gram[:half, :half]
    side = gram[:half, half:]
    lower = gram[half:, half:]
    row = jnp.arange(half, dtype=jnp.int32)[:, None]
    col = jnp.arange(half, dtype=jnp.int32)[None, :]
    keep_upper = row <= col
    merged = jnp.where(keep_upper, upper, lower)
    diagonal = jnp.diagonal(lower)[None, :]
    packed = chip_split_sum(jnp.concatenate([side, merged, diagonal], axis=0))
    side = packed[:half]
    merged = packed[half : 2 * half]
    diagonal = packed[2 * half]
    upper = jnp.where(keep_upper, merged, merged.T)
    lower = jnp.where(row > col, merged, merged.T)
    lower = jnp.where(row == col, diagonal[None, :], lower)
    return jnp.concatenate(
        [jnp.concatenate([upper, side], axis=1), jnp.concatenate([side.T, lower], axis=1)], axis=0
    )


def band_filter(gram_sum, clutter_rank, noise_rank, steps=9, coarse_steps=5):
    width = gram_sum.shape[0]
    identity = jnp.eye(width, dtype=jnp.float32)
    total_trace = jnp.sum(gram_sum * identity)
    levels = total_trace / jnp.stack([clutter_rank, noise_rank]).astype(jnp.float32)
    shifted = gram_sum[None] + levels[:, None, None] * identity[None]
    scale = 2.0 / (2.0 * levels + total_trace)
    inverse = scale[:, None, None] * identity[None]
    low = scale * levels

    def refine(precision):
        def step(_, carry):
            inverse, low = carry
            squeezed = low * (2.0 - low)
            factor = 2.0 / (1.0 + squeezed)
            product = jnp.einsum("bij,bjk->bik", shifted, inverse, precision=precision)
            inverse = factor[:, None, None] * (
                2.0 * inverse - jnp.einsum("bij,bjk->bik", inverse, product, precision=precision)
            )
            return inverse, factor * squeezed

        return step

    carry = lax.fori_loop(0, coarse_steps, refine(lax.Precision.HIGH), (inverse, low))
    inverse, _ = lax.fori_loop(coarse_steps, steps, refine(lax.Precision.HIGHEST), carry)
    resolvents = levels[:, None, None] * inverse
    return resolvents[0] - resolvents[1]


def body(volume, lat_taps, elev_taps, time_taps, clutter_rank, noise_rank):
    lat_count, elev_count, depth, columns = volume.shape
    matrix = time_matrix(time_taps, columns // 2)
    extended = halo_pieces(volume, 3)
    row_block = filtered_rows(extended, lat_taps, elev_taps, matrix)
    local_gram = lax.dot_general(
        row_block, row_block, (((0,), (0,)), ((), ())), preferred_element_type=jnp.float32
    )
    gram_sum = packed_gram_sum(local_gram)
    weights = band_filter(gram_sum, clutter_rank, noise_rank)
    cleaned_rows = jnp.dot(
        row_block, weights.astype(jnp.bfloat16), preferred_element_type=jnp.float32
    ).astype(jnp.bfloat16)
    cleaned = cleaned_rows.reshape(lat_count, elev_count, depth, columns)
    power = jnp.sum(jnp.square(cleaned.astype(jnp.float32)), axis=3)
    return (cleaned, power, weights)


def solution(mesh):
    placed = (P("lat", "elev", None, None), P(), P(), P(), P(), P())
    return jax.shard_map(
        body,
        mesh=mesh,
        in_specs=placed,
        out_specs=(P("lat", "elev", None, None), P("lat", "elev", None), P()),
        check_vma=False,
    )
```

```python
import jax
import jax.numpy as jnp
from jax import lax
from jax.experimental import pallas as pl
from jax.experimental.pallas import tpu as pltpu
from jax.sharding import PartitionSpec as P


def halo_pieces(block, width):
    lat_size, elev_size = block.shape[0], block.shape[1]
    low_lat = slice(lat_size - width, lat_size)
    high_lat = slice(0, width)
    low_elev = slice(elev_size - width, elev_size)
    high_elev = slice(0, width)

    def shift(piece, axis, step):
        count = lax.axis_size(axis)
        pairs = [(i, i + step) for i in range(count) if 0 <= i + step < count]
        return lax.ppermute(piece, axis, pairs)

    north = shift(block[low_lat], "lat", 1)
    south = shift(block[high_lat], "lat", -1)
    west = shift(block[:, low_elev], "elev", 1)
    east = shift(block[:, high_elev], "elev", -1)
    north_west = shift(west[low_lat], "lat", 1)
    north_east = shift(east[low_lat], "lat", 1)
    south_west = shift(west[high_lat], "lat", -1)
    south_east = shift(east[high_lat], "lat", -1)
    center = (block, north, south)
    left = (north_west, west, south_west)
    right = (north_east, east, south_east)
    return left, center, right


def time_matrix(time_taps, frames):
    count_taps = time_taps.shape[0]
    source = jnp.arange(frames, dtype=jnp.int32)[:, None]
    target = jnp.arange(frames, dtype=jnp.int32)[None, :]
    lagged = target - source
    matched = lagged[:, :, None] == jnp.arange(count_taps, dtype=jnp.int32)[None, None, :]
    single = jnp.sum(
        jnp.where(matched, time_taps.astype(jnp.float32)[None, None, :], jnp.float32(0.0)), axis=2
    )
    paired = jnp.kron(jnp.eye(2, dtype=jnp.float32), single)
    return paired.astype(jnp.bfloat16)


def lat_rows(rows, lat_taps, lat_count):
    sums = []
    for l in range(lat_count):
        total = lat_taps[0] * rows[l]
        for i in range(1, 7):
            total = total + lat_taps[i] * rows[l + i]
        sums.append(total)
    return sums


def center_smooth_kernel(lat_ref, elev_ref, block_ref, north_ref, south_ref, out_ref):
    lat_taps = [lat_ref[i] for i in range(7)]
    elev_taps = [elev_ref[i] for i in range(7)]
    lat_count, elev_count = out_ref.shape[0], out_ref.shape[1]
    refs = (north_ref, block_ref, south_ref)
    rows = [ref[k].astype(jnp.float32) for ref in refs for k in range(ref.shape[0])]
    for l, row in enumerate(lat_rows(rows, lat_taps, lat_count)):
        for e in range(elev_count):
            taps = [j for j in range(7) if 0 <= e + j - 3 < elev_count]
            total = elev_taps[taps[0]] * row[e + taps[0] - 3]
            for j in taps[1:]:
                total = total + elev_taps[j] * row[e + j - 3]
            out_ref[l, e] = total


def edge_smooth_kernel(lat_ref, elev_ref, middle_ref, *refs):
    out_ref = refs[-1]
    left_refs, right_refs = refs[0:3], refs[3:6]
    lat_taps = [lat_ref[i] for i in range(7)]
    elev_taps = [elev_ref[i] for i in range(7)]
    lat_count, elev_count = out_ref.shape[0], out_ref.shape[1]
    width = left_refs[0].shape[1]

    def side_rows(side_refs):
        rows = [ref[k].astype(jnp.float32) for ref in side_refs for k in range(ref.shape[0])]
        return lat_rows(rows, lat_taps, lat_count)

    left = side_rows(left_refs)
    right = side_rows(right_refs)
    for l in range(lat_count):
        for e in range(elev_count):
            total = middle_ref[l, e]
            for j in range(7):
                column = e + j
                if column < width:
                    total = total + elev_taps[j] * left[l][column]
                elif column >= width + elev_count:
                    total = total + elev_taps[j] * right[l][column - width - elev_count]
            out_ref[l, e] = total.astype(out_ref.dtype)


def tiled_call(kernel, pieces, out_dtype, lat_taps, elev_taps, tile=32):
    _, _, depth, columns = pieces[0].shape
    tile = tile if depth % tile == 0 else depth
    smem = pl.BlockSpec(memory_space=pltpu.SMEM)

    def tiled(piece):
        return pl.BlockSpec((piece.shape[0], piece.shape[1], tile, columns), lambda k: (0, 0, k, 0))

    return pl.pallas_call(
        kernel,
        out_shape=jax.ShapeDtypeStruct(pieces[0].shape, out_dtype),
        grid=(depth // tile,),
        in_specs=[smem, smem, *[tiled(piece) for piece in pieces]],
        out_specs=tiled(pieces[0]),
        interpret=INTERPRET,
    )(lat_taps, elev_taps, *pieces)


INTERPRET = False


def smooth(pieces, lat_taps, elev_taps):
    left, center, right = pieces
    middle = tiled_call(center_smooth_kernel, center, jnp.float32, lat_taps, elev_taps)
    return tiled_call(edge_smooth_kernel, (middle, *left, *right), jnp.bfloat16, lat_taps, elev_taps, tile=64)


def filtered_rows(pieces, lat_taps, elev_taps, matrix):
    smoothed = smooth(pieces, lat_taps, elev_taps)
    flat_rows = smoothed.reshape(-1, matrix.shape[0])
    return jnp.dot(flat_rows, matrix, preferred_element_type=jnp.float32).astype(jnp.bfloat16)


def butterfly_sum(block, groups):
    for axis, strides in groups:
        count = lax.axis_size(axis)
        received = []
        for mask in strides:
            if mask < count:
                received.append(lax.ppermute(block, axis, [(i, i ^ mask) for i in range(count)]))
        if len(received) == 3:
            block = (block + received[0]) + (received[1] + received[2])
        elif received:
            block = block + received[0]
    return block


def radix_groups(axis, first):
    count = lax.axis_size(axis)
    groups = []
    stride = first
    while stride < count:
        if 2 * stride < count:
            groups.append((axis, (stride, 2 * stride, 3 * stride)))
            stride *= 4
        else:
            groups.append((axis, (stride,)))
            stride *= 2
    return groups


def chip_split_sum(block):
    rows = block.shape[0]
    padded_rows = -(-rows // 16) * 16
    block = jnp.pad(block, ((0, padded_rows - rows), (0, 0)))
    swap = [(i, i ^ 1) for i in range(lax.axis_size("lat"))]
    block = block + lax.ppermute(block, "lat", swap)
    half = padded_rows // 2
    core = lax.axis_index("lat") % 2
    own = lax.dynamic_slice_in_dim(block, core * half, half, axis=0)
    own = butterfly_sum(own, radix_groups("lat", 2) + radix_groups("elev", 1))
    other = lax.ppermute(own, "lat", swap)
    first = jnp.where(core == 0, own, other)
    second = jnp.where(core == 0, other, own)
    return jnp.concatenate([first, second], axis=0)[:rows]


def packed_gram_sum(gram):
    half = gram.shape[0] // 2
    upper = gram[:half, :half]
    side = gram[:half, half:]
    lower = gram[half:, half:]
    row = jnp.arange(half, dtype=jnp.int32)[:, None]
    col = jnp.arange(half, dtype=jnp.int32)[None, :]
    keep_upper = row <= col
    merged = jnp.where(keep_upper, upper, lower)
    diagonal = jnp.diagonal(lower)[None, :]
    packed = chip_split_sum(jnp.concatenate([side, merged, diagonal], axis=0))
    side = packed[:half]
    merged = packed[half : 2 * half]
    diagonal = packed[2 * half]
    upper = jnp.where(keep_upper, merged, merged.T)
    lower = jnp.where(row > col, merged, merged.T)
    lower = jnp.where(row == col, diagonal[None, :], lower)
    return jnp.concatenate(
        [jnp.concatenate([upper, side], axis=1), jnp.concatenate([side.T, lower], axis=1)], axis=0
    )


def band_filter(gram_sum, clutter_rank, noise_rank, steps=8, coarse_steps=5):
    width = gram_sum.shape[0]
    identity = jnp.eye(width, dtype=jnp.float32)
    total_trace = jnp.sum(gram_sum * identity)
    levels = total_trace / jnp.stack([clutter_rank, noise_rank]).astype(jnp.float32)
    shifted = gram_sum[None] + levels[:, None, None] * identity[None]
    scale = 2.0 / (2.0 * levels + total_trace)
    inverse = scale[:, None, None] * identity[None]
    low = scale * levels

    def refine(precision):
        def step(_, carry):
            inverse, low = carry
            squeezed = low * (2.0 - low)
            factor = 2.0 / (1.0 + squeezed)
            product = jnp.einsum("bij,bjk->bik", shifted, inverse, precision=precision)
            inverse = factor[:, None, None] * (
                2.0 * inverse - jnp.einsum("bij,bjk->bik", inverse, product, precision=precision)
            )
            return inverse, factor * squeezed

        return step

    carry = lax.fori_loop(0, coarse_steps, refine(lax.Precision.HIGH), (inverse, low))
    inverse, _ = lax.fori_loop(coarse_steps, steps, refine(lax.Precision.HIGHEST), carry)
    resolvents = levels[:, None, None] * inverse
    return resolvents[0] - resolvents[1]


def body(volume, lat_taps, elev_taps, time_taps, clutter_rank, noise_rank):
    lat_count, elev_count, depth, columns = volume.shape
    matrix = time_matrix(time_taps, columns // 2)
    extended = halo_pieces(volume, 3)
    row_block = filtered_rows(extended, lat_taps, elev_taps, matrix)
    local_gram = lax.dot_general(
        row_block, row_block, (((0,), (0,)), ((), ())), preferred_element_type=jnp.float32
    )
    gram_sum = packed_gram_sum(local_gram)
    weights = band_filter(gram_sum, clutter_rank, noise_rank)
    cleaned_rows = jnp.dot(
        row_block, weights.astype(jnp.bfloat16), preferred_element_type=jnp.float32
    ).astype(jnp.bfloat16)
    cleaned = cleaned_rows.reshape(lat_count, elev_count, depth, columns)
    power = jnp.sum(jnp.square(cleaned.astype(jnp.float32)), axis=3)
    return (cleaned, power, weights)


def solution(mesh):
    placed = (P("lat", "elev", None, None), P(), P(), P(), P(), P())
    return jax.shard_map(
        body,
        mesh=mesh,
        in_specs=placed,
        out_specs=(P("lat", "elev", None, None), P("lat", "elev", None), P()),
        check_vma=False,
    )
```
